512 devices in a mesh: tm: 32 (over z, x_lo), recv: 16 (over x_hi, y, core).
Axes of the slice: x: 4 (x_hi: 2, x_lo: 2; x = x_hi * 2 + x_lo), y: 4, z: 16, core: 2. Of those that a mesh axis runs over, the one named last changes fastest.
Arguments:
- traces: bfloat16 [128, 4096, 2048], P('tm', 'recv'), may hold values from -6 to 6
- valid: int32 [128, 4096], P('tm', 'recv'), may hold values 0 or 1
- src_idx: int32 [32], replicated, may hold values from 0 to 4095
Outputs:
- stacks: float32 [32, 2, 61, 4096], P('tm', None, None, 'recv')
The draws below stay inside these ranges and needn't reach their ends.
All inputs are finite; a program needn't handle non-finite values. No bound on the sum of `valid` on one device may be relied on, other than what follows from the above.
Results may differ from the reference program's by a relative error of at most 0.0035.
Values sent between devices are 32-bit elements; how exact they have to be, the bound alone decides.
No kernel may reach another device: no remote copies, remote signals or barrier semaphores. Data moves between devices by JAX's collectives and lax.ppermute only.
A program may use at most 64 MiB of HBM per device.

```python
import math
import jax
import jax.numpy as jnp
from jax import lax

NS = 2048
NB = 61
BIN0 = 40
NSRC = 32
SEGMENTS = 128
CHANNELS = 4096


def set_ends(values, stream_key, smallest, top_value):
    longest = values.shape.index(max(values.shape))
    spots = []
    for shift in (0, 1):
        where = [jax.random.randint(jax.random.fold_in(stream_key, axis), (), 0, length) for axis, length in enumerate(values.shape)]
        where[longest] = (where[longest] + shift) % values.shape[longest]
        spots.append(tuple(where))
    return values.at[spots[0]].set(smallest).at[spots[1]].set(top_value)


def block_levels(own_key, shape, cuts, least, top_value):
    level, own = 1.0, jax.random.fold_in(own_key, 6)
    for position, parts in cuts:
        draws = jnp.exp(jax.random.uniform(jax.random.fold_in(own, position), (parts,), jnp.float32, least / len(cuts), top_value / len(cuts)))
        level = level * jnp.repeat(draws, shape[position] // parts).reshape([-1 if axis == position else 1 for axis in range(len(shape))])
    return level


def gaussian(rng, shape, width, most, cuts=(), kind=jnp.bfloat16):
    entries = width * jax.random.normal(rng, shape, jnp.float32)
    if cuts:
        entries = entries * block_levels(rng, shape, cuts, -0.22, 0.18)
    return jnp.clip(entries, -most, most).astype(kind)


def setup_inputs(seed: int = 0) -> dict:
    key_of = jax.random.split(jax.random.key(seed), 4)
    return {
        "traces": gaussian(key_of[0], (SEGMENTS, CHANNELS, NS), 1.0, 6.0, ((0, 32), (1, 16))),
        "valid": set_ends((jax.random.randint(key_of[1], (SEGMENTS, CHANNELS), 0, 8) < 7).astype(jnp.int32), jax.random.fold_in(key_of[1], 1), 0, 1),
        "src_idx": set_ends(jax.random.randint(key_of[2], (NSRC,), 0, CHANNELS), jax.random.fold_in(key_of[2], 1), 0, CHANNELS - 1).astype(jnp.int32),
    }


def basis_table():
    sample_ids = jnp.arange(NS, dtype=jnp.int32)
    bin_ids = BIN0 + jnp.arange(NB, dtype=jnp.int32)
    phase_ids = bin_ids[:, None] * sample_ids[None, :] % NS
    angle = 2.0 * math.pi / NS * phase_ids.astype(jnp.float32)
    return jnp.concatenate([jnp.cos(angle), -jnp.sin(angle)], axis=0).astype(jnp.bfloat16)

def whiten_block(spec, valid_float):
    real_part = spec[:NB]
    imag_part = spec[NB:]
    power = real_part * real_part + imag_part * imag_part
    level = lax.optimization_barrier(jnp.sum(power, axis=0)) / (2.0 * NB)
    scale = lax.rsqrt(power + level[None] + 1e-06) * valid_float[None]
    return jnp.concatenate([real_part * scale, imag_part * scale], axis=0)

def reference(traces, valid, src_idx):
    basis = basis_table()
    valid_float = valid.astype(jnp.float32)

    def one_segment(totals, inputs):
        segment, seg_valid = inputs
        spec = lax.dot_general(basis, segment, (((1,), (1,)), ((), ())), preferred_element_type=jnp.float32)
        white = whiten_block(spec, seg_valid)
        panel = white[:, src_idx]
        src_real = panel[:NB]
        src_imag = panel[NB:]
        own_real = white[:NB]
        own_imag = white[NB:]
        real_sum = src_real.T[:, :, None] * own_real[None] + src_imag.T[:, :, None] * own_imag[None]
        imag_sum = src_real.T[:, :, None] * own_imag[None] - src_imag.T[:, :, None] * own_real[None]
        return (totals + jnp.stack([real_sum, imag_sum], axis=1), None)
    start_sum = jnp.zeros((NSRC, 2, NB, traces.shape[1]), jnp.float32)
    totals, _ = lax.scan(one_segment, start_sum, (traces, valid_float))
    return totals / jnp.sqrt(jnp.float32(traces.shape[0]))
```

```python
import math

import jax
import jax.numpy as jnp
import numpy as np
from jax import lax
from jax.sharding import Mesh
from jax.sharding import PartitionSpec as P

NS = 2048
NB = 61
BIN0 = 40
NB_PAD = 64


def basis_table():
    sample_ids = jnp.arange(NS, dtype=jnp.int32)
    bin_ids = BIN0 + jnp.arange(NB, dtype=jnp.int32)
    phase_ids = bin_ids[:, None] * sample_ids[None, :] % NS
    angle = 2.0 * math.pi / NS * phase_ids.astype(jnp.float32)
    return jnp.concatenate([jnp.cos(angle), -jnp.sin(angle)], axis=0).astype(jnp.bfloat16)


def whiten_block(spec, valid_float):
    real_part = spec[:NB]
    imag_part = spec[NB:]
    power = real_part * real_part + imag_part * imag_part
    level = jnp.sum(power, axis=0) / (2.0 * NB)
    scale = lax.rsqrt(power + level[None] + 1e-06) * valid_float[None]
    return jnp.concatenate([real_part * scale, imag_part * scale], axis=0)


def pad_bins(part):
    return jnp.pad(part, [(0, NB_PAD - NB)] + [(0, 0)] * (part.ndim - 1))


def cross_terms(panel, white, factor):
    high = lax.Precision.HIGHEST
    src_real = pad_bins(panel[:NB])
    src_imag = pad_bins(panel[NB:])
    own_real = pad_bins(white[:NB])
    own_imag = pad_bins(white[NB:])
    real_sum = jnp.einsum("fts,ftc->sfc", src_real, own_real, precision=high) + jnp.einsum(
        "fts,ftc->sfc", src_imag, own_imag, precision=high
    )
    imag_sum = jnp.einsum("fts,ftc->sfc", src_real, own_imag, precision=high) - jnp.einsum(
        "fts,ftc->sfc", src_imag, own_real, precision=high
    )
    return jnp.stack([real_sum, imag_sum], axis=1) * factor


def psum_recv(value, size):
    bit = 1
    while bit < size:
        pairs = [(i, i ^ bit) for i in range(size)]
        value = value + lax.ppermute(value, "recv", pairs)
        bit *= 2
    return value


def on_device(traces, valid, src_idx):
    seg_count = traces.shape[0]
    chan_count = traces.shape[1]
    pair = lax.axis_size("xlo")
    total_segs = seg_count * pair * lax.axis_size("z")
    basis = basis_table()
    valid_float = valid.astype(jnp.float32)
    offset = lax.axis_index("recv") * chan_count
    onehot = (src_idx[:, None] == offset + jnp.arange(chan_count, dtype=jnp.int32)[None, :]).astype(
        jnp.float32
    )
    spec = lax.dot_general(
        basis, traces, (((1,), (2,)), ((), ())), preferred_element_type=jnp.float32
    )
    white = whiten_block(spec, valid_float)
    partial_value = jnp.einsum("ktc,sc->kts", white, onehot, precision=lax.Precision.HIGHEST)
    panel = psum_recv(partial_value, lax.axis_size("recv"))
    white_pair = lax.all_gather(white, "xlo", axis=1, tiled=True)
    panel_pair = lax.all_gather(panel, "xlo", axis=1, tiled=True)
    nsrc = panel_pair.shape[2]
    panel_pair = panel_pair.reshape(panel_pair.shape[0], panel_pair.shape[1], nsrc // pair, pair)
    panel_own = lax.dynamic_index_in_dim(panel_pair, lax.axis_index("xlo"), axis=3, keepdims=False)
    factor = 1.0 / math.sqrt(total_segs)
    totals = cross_terms(panel_own, white_pair, factor)
    out = lax.psum_scatter(totals, "z", scatter_dimension=0, tiled=True)
    return out[:, :, :NB, :]


def solution(mesh):
    tm_size = mesh.shape["tm"]
    recv_size = mesh.shape["recv"]
    devices = np.asarray(mesh.devices).reshape(tm_size // 2, 2, recv_size)
    inner = Mesh(devices, ("z", "xlo", "recv"))
    return jax.shard_map(
        on_device,
        mesh=inner,
        in_specs=(P(("z", "xlo"), "recv", None), P(("z", "xlo"), "recv"), P()),
        out_specs=P(("z", "xlo"), None, None, "recv"),
        check_vma=False,
    )
```

```python
import math

import jax
import jax.numpy as jnp
import numpy as np
from jax import lax
from jax.sharding import Mesh
from jax.sharding import PartitionSpec as P

NS = 2048
NB = 61
BIN0 = 40
NB_PAD = 64


def basis_table():
    sample_ids = jnp.arange(NS, dtype=jnp.int32)
    bin_ids = BIN0 + jnp.arange(NB, dtype=jnp.int32)
    phase_ids = bin_ids[:, None] * sample_ids[None, :] % NS
    angle = 2.0 * math.pi / NS * phase_ids.astype(jnp.float32)
    return jnp.concatenate([jnp.cos(angle), -jnp.sin(angle)], axis=0).astype(jnp.bfloat16)


def whiten_block(spec, valid_float):
    real_part = spec[:NB]
    imag_part = spec[NB:]
    power = real_part * real_part + imag_part * imag_part
    level = jnp.sum(power, axis=0) / (2.0 * NB)
    scale = lax.rsqrt(power + level[None] + 1e-06) * valid_float[None]
    return jnp.concatenate([real_part * scale, imag_part * scale], axis=0)


def pad_bins(part):
    return jnp.pad(part, [(0, NB_PAD - NB)] + [(0, 0)] * (part.ndim - 1))


def cross_terms(panel, white, factor):
    high = lax.Precision.HIGHEST
    src_real = pad_bins(panel[:NB])
    src_imag = pad_bins(panel[NB:])
    own_real = pad_bins(white[:NB])
    own_imag = pad_bins(white[NB:])
    real_sum = jnp.einsum("fts,ftc->sfc", src_real, own_real, precision=high) + jnp.einsum(
        "fts,ftc->sfc", src_imag, own_imag, precision=high
    )
    imag_sum = jnp.einsum("fts,ftc->sfc", src_real, own_imag, precision=high) - jnp.einsum(
        "fts,ftc->sfc", src_imag, own_real, precision=high
    )
    return jnp.stack([real_sum, imag_sum], axis=1) * factor


def psum_recv(value, size):
    bit = 1
    while bit < size:
        pairs = [(i, i ^ bit) for i in range(size)]
        value = value + lax.ppermute(value, "recv", pairs)
        bit *= 2
    return value


def on_device(traces, valid, src_idx):
    seg_count = traces.shape[0]
    chan_count = traces.shape[1]
    pair = lax.axis_size("xlo")
    total_segs = seg_count * pair * lax.axis_size("z")
    basis = basis_table()
    valid_float = valid.astype(jnp.float32)
    offset = lax.axis_index("recv") * chan_count
    onehot = (src_idx[:, None] == offset + jnp.arange(chan_count, dtype=jnp.int32)[None, :]).astype(
        jnp.float32
    )
    spec = lax.dot_general(
        basis, traces, (((1,), (2,)), ((), ())), preferred_element_type=jnp.float32
    )
    white = whiten_block(spec, valid_float)
    partial_value = jnp.einsum("ktc,sc->kts", white, onehot, precision=lax.Precision.HIGHEST)
    panel = psum_recv(partial_value, lax.axis_size("recv"))
    swap = [(0, 1), (1, 0)]
    mine = lax.axis_index("xlo")
    white_pair = jnp.concatenate([white, lax.ppermute(white, "xlo", swap)], axis=1)
    nsrc = panel.shape[2]
    panel = panel.reshape(panel.shape[0], panel.shape[1], nsrc // pair, pair)
    panel_mine = lax.dynamic_index_in_dim(panel, mine, axis=3, keepdims=False)
    panel_theirs = lax.dynamic_index_in_dim(panel, 1 - mine, axis=3, keepdims=False)
    panel_own = jnp.concatenate([panel_mine, lax.ppermute(panel_theirs, "xlo", swap)], axis=1)
    factor = 1.0 / math.sqrt(total_segs)
    totals = cross_terms(panel_own, white_pair, factor)
    out = lax.psum_scatter(totals, "z", scatter_dimension=0, tiled=True)
    return out[:, :, :NB, :]


def solution(mesh):
    tm_size = mesh.shape["tm"]
    recv_size = mesh.shape["recv"]
    devices = np.asarray(mesh.devices).reshape(tm_size // 2, 2, recv_size)
    inner = Mesh(devices, ("z", "xlo", "recv"))
    return jax.shard_map(
        on_device,
        mesh=inner,
        in_specs=(P(("z", "xlo"), "recv", None), P(("z", "xlo"), "recv"), P()),
        out_specs=P(("z", "xlo"), None, None, "recv"),
        check_vma=False,
    )
```

```python
import math

import jax
import jax.numpy as jnp
import numpy as np
from jax import lax
from jax.sharding import Mesh
from jax.sharding import PartitionSpec as P

NS = 2048
NB = 61
BIN0 = 40
NB_PAD = 64


def basis_table():
    sample_ids = jnp.arange(NS, dtype=jnp.int32)
    bin_ids = BIN0 + jnp.arange(NB, dtype=jnp.int32)
    phase_ids = bin_ids[:, None] * sample_ids[None, :] % NS
    angle = 2.0 * math.pi / NS * phase_ids.astype(jnp.float32)
    return jnp.concatenate([jnp.cos(angle), -jnp.sin(angle)], axis=0).astype(jnp.bfloat16)


def whiten_block(spec, valid_float):
    real_part = spec[:NB]
    imag_part = spec[NB:]
    power = real_part * real_part + imag_part * imag_part
    level = jnp.sum(power, axis=0) / (2.0 * NB)
    scale = lax.rsqrt(power + level[None] + 1e-06) * valid_float[None]
    return jnp.concatenate([real_part * scale, imag_part * scale], axis=0)


def pad_bins(part):
    return jnp.pad(part, [(0, NB_PAD - NB)] + [(0, 0)] * (part.ndim - 1))


def cross_terms(panel, white, factor):
    high = lax.Precision.HIGHEST
    src_real = pad_bins(panel[:NB])
    src_imag = pad_bins(panel[NB:])
    own_real = pad_bins(white[:NB])
    own_imag = pad_bins(white[NB:])
    real_sum = jnp.einsum("fts,ftc->sfc", src_real, own_real, precision=high) + jnp.einsum(
        "fts,ftc->sfc", src_imag, own_imag, precision=high
    )
    imag_sum = jnp.einsum("fts,ftc->sfc", src_real, own_imag, precision=high) - jnp.einsum(
        "fts,ftc->sfc", src_imag, own_real, precision=high
    )
    return jnp.stack([real_sum, imag_sum], axis=1) * factor


def psum_recv(value, size):
    bit = 1
    while bit < size:
        pairs = [(i, i ^ bit) for i in range(size)]
        value = value + lax.ppermute(value, "recv", pairs)
        bit *= 2
    return value


def on_device(traces, valid, src_idx):
    seg_count = traces.shape[0]
    chan_count = traces.shape[1]
    group = ("zlo", "xlo")
    width = lax.axis_size("zlo") * lax.axis_size("xlo")
    total_segs = seg_count * width * lax.axis_size("zhi")
    basis = basis_table()
    valid_float = valid.astype(jnp.float32)
    offset = lax.axis_index("recv") * chan_count
    onehot = (src_idx[:, None] == offset + jnp.arange(chan_count, dtype=jnp.int32)[None, :]).astype(
        jnp.float32
    )
    spec = lax.dot_general(
        basis, traces, (((1,), (2,)), ((), ())), preferred_element_type=jnp.float32
    )
    white = whiten_block(spec, valid_float)
    q = lax.axis_index("zlo") * lax.axis_size("xlo") + lax.axis_index("xlo")
    moves = [[(r, r ^ b) for r in range(width)] for b in range(1, width)]
    white_all = jnp.concatenate(
        [white] + [lax.ppermute(white, group, pairs) for pairs in moves], axis=1
    )
    partial_value = jnp.einsum("ktc,sc->kts", white, onehot, precision=lax.Precision.HIGHEST)
    panel = psum_recv(partial_value, lax.axis_size("recv"))
    nsrc = panel.shape[2]
    panel = panel.reshape(panel.shape[0], panel.shape[1], nsrc // width, width)
    blocks = [lax.dynamic_index_in_dim(panel, q, axis=3, keepdims=False)]
    for b, pairs in zip(range(1, width), moves):
        theirs = lax.dynamic_index_in_dim(panel, q ^ b, axis=3, keepdims=False)
        blocks.append(lax.ppermute(theirs, group, pairs))
    panel_own = jnp.concatenate(blocks, axis=1)
    factor = 1.0 / math.sqrt(total_segs)
    totals = cross_terms(panel_own, white_all, factor)
    out = lax.psum_scatter(totals, "zhi", scatter_dimension=0, tiled=True)
    return out[:, :, :NB, :]


def solution(mesh):
    tm_size = mesh.shape["tm"]
    recv_size = mesh.shape["recv"]
    devices = np.asarray(mesh.devices).reshape(tm_size // 4, 2, 2, recv_size)
    inner = Mesh(devices, ("zhi", "zlo", "xlo", "recv"))
    return jax.shard_map(
        on_device,
        mesh=inner,
        in_specs=(P(("zhi", "zlo", "xlo"), "recv", None), P(("zhi", "zlo", "xlo"), "recv"), P()),
        out_specs=P(("zhi", "zlo", "xlo"), None, None, "recv"),
        check_vma=False,
    )
```

```python
import math

import jax
import jax.numpy as jnp
import numpy as np
from jax import lax
from jax.sharding import Mesh
from jax.sharding import PartitionSpec as P

NS = 2048
NB = 61
BIN0 = 40
NB_PAD = 64


def basis_table():
    sample_ids = jnp.arange(NS, dtype=jnp.int32)
    bin_ids = BIN0 + jnp.arange(NB, dtype=jnp.int32)
    phase_ids = bin_ids[:, None] * sample_ids[None, :] % NS
    angle = 2.0 * math.pi / NS * phase_ids.astype(jnp.float32)
    return jnp.concatenate([jnp.cos(angle), -jnp.sin(angle)], axis=0).astype(jnp.bfloat16)


def whiten_block(spec, valid_float):
    real_part = spec[:NB]
    imag_part = spec[NB:]
    power = real_part * real_part + imag_part * imag_part
    level = jnp.sum(power, axis=0) / (2.0 * NB)
    scale = lax.rsqrt(power + level[None] + 1e-06) * valid_float[None]
    return jnp.concatenate([real_part * scale, imag_part * scale], axis=0)


def pad_bins(part):
    return jnp.pad(part, [(0, NB_PAD - NB)] + [(0, 0)] * (part.ndim - 1))


def cross_terms(panel, white, factor):
    high = lax.Precision.HIGHEST
    src_real = pad_bins(panel[:NB])
    src_imag = pad_bins(panel[NB:])
    own_real = pad_bins(white[:NB])
    own_imag = pad_bins(white[NB:])
    real_sum = jnp.einsum("fts,ftc->sfc", src_real, own_real, precision=high) + jnp.einsum(
        "fts,ftc->sfc", src_imag, own_imag, precision=high
    )
    imag_sum = jnp.einsum("fts,ftc->sfc", src_real, own_imag, precision=high) - jnp.einsum(
        "fts,ftc->sfc", src_imag, own_real, precision=high
    )
    return jnp.stack([real_sum, imag_sum], axis=1) * factor


def psum_recv(value, size):
    bit = 1
    while bit < size:
        pairs = [(i, i ^ bit) for i in range(size)]
        value = value + lax.ppermute(value, "recv", pairs)
        bit *= 2
    return value


def on_device(traces, valid, src_idx):
    seg_count = traces.shape[0]
    chan_count = traces.shape[1]
    group = ("zlo", "xlo")
    width = lax.axis_size("zlo") * lax.axis_size("xlo")
    total_segs = seg_count * width * lax.axis_size("zhi")
    basis = basis_table()
    valid_float = valid.astype(jnp.float32)
    offset = lax.axis_index("recv") * chan_count
    onehot = (src_idx[:, None] == offset + jnp.arange(chan_count, dtype=jnp.int32)[None, :]).astype(
        jnp.float32
    )
    spec = lax.dot_general(
        basis, traces, (((1,), (2,)), ((), ())), preferred_element_type=jnp.float32
    )
    white = whiten_block(spec, valid_float)
    q = lax.axis_index("zlo") * lax.axis_size("xlo") + lax.axis_index("xlo")
    moves = [[(r, r ^ b) for r in range(width)] for b in range(1, width)]
    partial_value = jnp.einsum("ktc,sc->kts", white, onehot, precision=lax.Precision.HIGHEST)
    nsrc = partial_value.shape[2]
    partial_value = partial_value.reshape(
        partial_value.shape[0], partial_value.shape[1], nsrc // width, width
    )
    white_parts = [white]
    value_parts = [lax.dynamic_index_in_dim(partial_value, q, axis=3, keepdims=False)]
    for b, pairs in zip(range(1, width), moves):
        theirs = lax.dynamic_index_in_dim(partial_value, q ^ b, axis=3, keepdims=False)
        got_white, got_value = lax.ppermute((white, theirs), group, pairs)
        white_parts.append(got_white)
        value_parts.append(got_value)
    white_parts, value_parts = lax.optimization_barrier((white_parts, value_parts))
    white_all = jnp.concatenate(white_parts, axis=1)
    panel_own = psum_recv(jnp.concatenate(value_parts, axis=1), lax.axis_size("recv"))
    factor = 1.0 / math.sqrt(total_segs)
    totals = cross_terms(panel_own, white_all, factor)
    out = lax.psum_scatter(totals, "zhi", scatter_dimension=0, tiled=True)
    return out[:, :, :NB, :]


def solution(mesh):
    tm_size = mesh.shape["tm"]
    recv_size = mesh.shape["recv"]
    devices = np.asarray(mesh.devices).reshape(tm_size // 4, 2, 2, recv_size)
    inner = Mesh(devices, ("zhi", "zlo", "xlo", "recv"))
    return jax.shard_map(
        on_device,
        mesh=inner,
        in_specs=(P(("zhi", "zlo", "xlo"), "recv", None), P(("zhi", "zlo", "xlo"), "recv"), P()),
        out_specs=P(("zhi", "zlo", "xlo"), None, None, "recv"),
        check_vma=False,
    )
```

```python
import math

import jax
import jax.numpy as jnp
import numpy as np
from jax import lax
from jax.sharding import Mesh
from jax.sharding import PartitionSpec as P

NS = 2048
NB = 61
BIN0 = 40
NB_PAD = 64


def basis_table():
    sample_ids = jnp.arange(NS, dtype=jnp.int32)
    bin_ids = BIN0 + jnp.arange(NB, dtype=jnp.int32)
    phase_ids = bin_ids[:, None] * sample_ids[None, :] % NS
    angle = 2.0 * math.pi / NS * phase_ids.astype(jnp.float32)
    return jnp.concatenate([jnp.cos(angle), -jnp.sin(angle)], axis=0).astype(jnp.bfloat16)


def whiten_block(spec, valid_float):
    real_part = spec[:NB]
    imag_part = spec[NB:]
    power = real_part * real_part + imag_part * imag_part
    level = jnp.sum(power, axis=0) / (2.0 * NB)
    scale = lax.rsqrt(power + level[None] + 1e-06) * valid_float[None]
    return jnp.concatenate([real_part * scale, imag_part * scale], axis=0)


def pad_bins(part):
    return jnp.pad(part, [(0, NB_PAD - NB)] + [(0, 0)] * (part.ndim - 1))


def cross_terms(panel, white, factor):
    high = lax.Precision.HIGHEST
    src_real = pad_bins(panel[:NB])
    src_imag = pad_bins(panel[NB:])
    own_real = pad_bins(white[:NB])
    own_imag = pad_bins(white[NB:])
    real_sum = jnp.einsum("fts,ftc->sfc", src_real, own_real, precision=high) + jnp.einsum(
        "fts,ftc->sfc", src_imag, own_imag, precision=high
    )
    imag_sum = jnp.einsum("fts,ftc->sfc", src_real, own_imag, precision=high) - jnp.einsum(
        "fts,ftc->sfc", src_imag, own_real, precision=high
    )
    return jnp.stack([real_sum, imag_sum], axis=1) * factor


def psum_recv(value, size, passengers, hold_bit):
    bit = 1
    while bit < size:
        if bit == hold_bit:
            value, passengers = lax.optimization_barrier((value, passengers))
        pairs = [(i, i ^ bit) for i in range(size)]
        value = value + lax.ppermute(value, "recv", pairs)
        bit *= 2
    return value, passengers


def on_device(traces, valid, src_idx):
    seg_count = traces.shape[0]
    chan_count = traces.shape[1]
    group = ("zlo", "xlo")
    width = lax.axis_size("zlo") * lax.axis_size("xlo")
    total_segs = seg_count * width * lax.axis_size("zhi")
    basis = basis_table()
    valid_float = valid.astype(jnp.float32)
    offset = lax.axis_index("recv") * chan_count
    onehot = (src_idx[:, None] == offset + jnp.arange(chan_count, dtype=jnp.int32)[None, :]).astype(
        jnp.float32
    )
    spec = lax.dot_general(
        basis, traces, (((1,), (2,)), ((), ())), preferred_element_type=jnp.float32
    )
    white = whiten_block(spec, valid_float)
    q = lax.axis_index("zlo") * lax.axis_size("xlo") + lax.axis_index("xlo")
    moves = [[(r, r ^ b) for r in range(width)] for b in range(1, width)]
    white_parts = [lax.ppermute(white, group, pairs) for pairs in moves]
    partial_value = jnp.einsum("ktc,sc->kts", white, onehot, precision=lax.Precision.HIGHEST)
    panel, white_parts = psum_recv(
        partial_value, lax.axis_size("recv"), white_parts, lax.axis_size("recv") // 2
    )
    white_all = jnp.concatenate([white] + white_parts, axis=1)
    nsrc = panel.shape[2]
    panel = panel.reshape(panel.shape[0], panel.shape[1], nsrc // width, width)
    blocks = [lax.dynamic_index_in_dim(panel, q, axis=3, keepdims=False)]
    for b, pairs in zip(range(1, width), moves):
        theirs = lax.dynamic_index_in_dim(panel, q ^ b, axis=3, keepdims=False)
        blocks.append(lax.ppermute(theirs, group, pairs))
    panel_own = jnp.concatenate(blocks, axis=1)
    factor = 1.0 / math.sqrt(total_segs)
    totals = cross_terms(panel_own, white_all, factor)
    out = lax.psum_scatter(totals, "zhi", scatter_dimension=0, tiled=True)
    return out[:, :, :NB, :]


def solution(mesh):
    tm_size = mesh.shape["tm"]
    recv_size = mesh.shape["recv"]
    devices = np.asarray(mesh.devices).reshape(tm_size // 4, 2, 2, recv_size)
    inner = Mesh(devices, ("zhi", "zlo", "xlo", "recv"))
    return jax.shard_map(
        on_device,
        mesh=inner,
        in_specs=(P(("zhi", "zlo", "xlo"), "recv", None), P(("zhi", "zlo", "xlo"), "recv"), P()),
        out_specs=P(("zhi", "zlo", "xlo"), None, None, "recv"),
        check_vma=False,
    )
```

```python
import math

import jax
import jax.numpy as jnp
import numpy as np
from jax import lax
from jax.sharding import Mesh
from jax.sharding import PartitionSpec as P

NS = 2048
NB = 61
BIN0 = 40
NB_PAD = 64


def basis_table():
    sample_ids = np.arange(NS, dtype=np.int64)
    bin_ids = BIN0 + np.arange(NB, dtype=np.int64)
    phase_ids = (bin_ids[:, None] * sample_ids[None, :] % NS).astype(np.float32)
    angle = (np.float32(2.0 * math.pi / NS) * phase_ids).astype(np.float64)
    table = np.concatenate([np.cos(angle), -np.sin(angle)], axis=0).astype(np.float32)
    return jnp.asarray(table.astype(jnp.bfloat16))


def whiten_block(spec, valid_float):
    real_part = spec[:NB]
    imag_part = spec[NB:]
    power = real_part * real_part + imag_part * imag_part
    level = jnp.sum(power, axis=0) / (2.0 * NB)
    scale = lax.rsqrt(power + level[None] + 1e-06) * valid_float[None]
    return jnp.concatenate([real_part * scale, imag_part * scale], axis=0)


def pad_bins(part):
    return jnp.pad(part, [(0, NB_PAD - NB)] + [(0, 0)] * (part.ndim - 1))


def cross_terms(panel, white, factor):
    high = lax.Precision.HIGHEST
    src_real = pad_bins(panel[:NB])
    src_imag = pad_bins(panel[NB:])
    own_real = pad_bins(white[:NB])
    own_imag = pad_bins(white[NB:])
    real_sum = jnp.einsum("fts,ftc->sfc", src_real, own_real, precision=high) + jnp.einsum(
        "fts,ftc->sfc", src_imag, own_imag, precision=high
    )
    imag_sum = jnp.einsum("fts,ftc->sfc", src_real, own_imag, precision=high) - jnp.einsum(
        "fts,ftc->sfc", src_imag, own_real, precision=high
    )
    return jnp.stack([real_sum, imag_sum], axis=1) * factor


def psum_recv(value, size, passengers, hold_bit):
    bit = 1
    while bit < size:
        if bit == hold_bit:
            value, passengers = lax.optimization_barrier((value, passengers))
        pairs = [(i, i ^ bit) for i in range(size)]
        value = value + lax.ppermute(value, "recv", pairs)
        bit *= 2
    return value, passengers


def on_device(traces, valid, src_idx):
    seg_count = traces.shape[0]
    chan_count = traces.shape[1]
    group = ("zlo", "xlo")
    width = lax.axis_size("zlo") * lax.axis_size("xlo")
    total_segs = seg_count * width * lax.axis_size("zhi")
    basis = basis_table()
    valid_float = valid.astype(jnp.float32)
    offset = lax.axis_index("recv") * chan_count
    onehot = (src_idx[:, None] == offset + jnp.arange(chan_count, dtype=jnp.int32)[None, :]).astype(
        jnp.float32
    )
    spec = lax.dot_general(
        basis, traces, (((1,), (2,)), ((), ())), preferred_element_type=jnp.float32
    )
    white = whiten_block(spec, valid_float)
    q = lax.axis_index("zlo") * lax.axis_size("xlo") + lax.axis_index("xlo")
    moves = [[(r, r ^ b) for r in range(width)] for b in range(1, width)]
    white_parts = [lax.ppermute(white, group, pairs) for pairs in moves]
    partial_value = jnp.einsum("ktc,sc->kts", white, onehot, precision=lax.Precision.HIGHEST)
    panel, white_parts = psum_recv(
        partial_value, lax.axis_size("recv"), white_parts, lax.axis_size("recv") // 2
    )
    white_all = jnp.concatenate([white] + white_parts, axis=1)
    nsrc = panel.shape[2]
    panel = panel.reshape(panel.shape[0], panel.shape[1], nsrc // width, width)
    blocks = [lax.dynamic_index_in_dim(panel, q, axis=3, keepdims=False)]
    for b, pairs in zip(range(1, width), moves):
        theirs = lax.dynamic_index_in_dim(panel, q ^ b, axis=3, keepdims=False)
        blocks.append(lax.ppermute(theirs, group, pairs))
    panel_own = jnp.concatenate(blocks, axis=1)
    factor = 1.0 / math.sqrt(total_segs)
    totals = cross_terms(panel_own, white_all, factor)
    out = lax.psum_scatter(totals, "zhi", scatter_dimension=0, tiled=True)
    return out[:, :, :NB, :]


def solution(mesh):
    tm_size = mesh.shape["tm"]
    recv_size = mesh.shape["recv"]
    devices = np.asarray(mesh.devices).reshape(tm_size // 4, 2, 2, recv_size)
    inner = Mesh(devices, ("zhi", "zlo", "xlo", "recv"))
    return jax.shard_map(
        on_device,
        mesh=inner,
        in_specs=(P(("zhi", "zlo", "xlo"), "recv", None), P(("zhi", "zlo", "xlo"), "recv"), P()),
        out_specs=P(("zhi", "zlo", "xlo"), None, None, "recv"),
        check_vma=False,
    )
```

```python
import math

import jax
import jax.numpy as jnp
import numpy as np
from jax import lax
from jax.sharding import Mesh
from jax.sharding import PartitionSpec as P

NS = 2048
NB = 61
BIN0 = 40
NB_PAD = 64


def basis_table():
    sample_ids = np.arange(NS, dtype=np.int64)
    bin_ids = BIN0 + np.arange(NB, dtype=np.int64)
    phase_ids = (bin_ids[:, None] * sample_ids[None, :] % NS).astype(np.float32)
    angle = (np.float32(2.0 * math.pi / NS) * phase_ids).astype(np.float64)
    table = np.concatenate([np.cos(angle), -np.sin(angle)], axis=0).astype(np.float32)
    return jnp.asarray(table.astype(jnp.bfloat16))


def whiten_block(spec, valid_float):
    real_part = spec[:NB]
    imag_part = spec[NB:]
    power = real_part * real_part + imag_part * imag_part
    level = jnp.sum(power, axis=0) / (2.0 * NB)
    scale = lax.rsqrt(power + level[None] + 1e-06) * valid_float[None]
    return jnp.concatenate([real_part * scale, imag_part * scale], axis=0)


def pad_bins(part):
    return jnp.pad(part, [(0, NB_PAD - NB)] + [(0, 0)] * (part.ndim - 1))


def cross_terms(panel, white, factor):
    high = lax.Precision.HIGHEST
    src_real = pad_bins(panel[:NB])
    src_imag = pad_bins(panel[NB:])
    own_real = pad_bins(white[:NB])
    own_imag = pad_bins(white[NB:])
    real_sum = jnp.einsum("fts,ftc->sfc", src_real, own_real, precision=high) + jnp.einsum(
        "fts,ftc->sfc", src_imag, own_imag, precision=high
    )
    imag_sum = jnp.einsum("fts,ftc->sfc", src_real, own_imag, precision=high) - jnp.einsum(
        "fts,ftc->sfc", src_imag, own_real, precision=high
    )
    return jnp.stack([real_sum, imag_sum], axis=1) * factor


def psum_recv(value, size):
    bit = 1
    while bit < size:
        pairs = [(i, i ^ bit) for i in range(size)]
        value = value + lax.ppermute(value, "recv", pairs)
        bit *= 2
    return value


def on_device(traces, valid, src_idx):
    seg_count = traces.shape[0]
    chan_count = traces.shape[1]
    group = ("zlo", "xlo")
    width = lax.axis_size("zlo") * lax.axis_size("xlo")
    total_segs = seg_count * width * lax.axis_size("zhi")
    basis = basis_table()
    valid_float = valid.astype(jnp.float32)
    offset = lax.axis_index("recv") * chan_count
    onehot = (src_idx[:, None] == offset + jnp.arange(chan_count, dtype=jnp.int32)[None, :]).astype(
        jnp.float32
    )
    spec = lax.dot_general(
        basis, traces, (((1,), (2,)), ((), ())), preferred_element_type=jnp.float32
    )
    white = whiten_block(spec, valid_float)
    q = lax.axis_index("zlo") * lax.axis_size("xlo") + lax.axis_index("xlo")
    moves = [[(r, r ^ b) for r in range(width)] for b in range(1, width)]
    partial_value = jnp.einsum("ktc,sc->kts", white, onehot, precision=lax.Precision.HIGHEST)
    rows, segs, nsrc = partial_value.shape
    partial_value = partial_value.reshape(rows, segs, nsrc // width, width)

    def slot(member):
        return lax.dynamic_index_in_dim(partial_value, member, axis=3, keepdims=False).reshape(rows, -1)

    slot_width = segs * (nsrc // width)
    white_parts = [white]
    value_parts = [slot(q)]
    for b, pairs in zip(range(1, width), moves):
        row = jnp.pad(slot(q ^ b), ((0, 0), (0, white.shape[2] - slot_width)))
        message = jnp.concatenate([white, row[:, None, :]], axis=1)
        got = lax.ppermute(message, group, pairs)
        white_parts.append(got[:, :segs, :])
        value_parts.append(got[:, segs, :slot_width])
    white_all = jnp.concatenate(white_parts, axis=1)
    panel = psum_recv(jnp.concatenate(value_parts, axis=1), lax.axis_size("recv"))
    panel_own = panel.reshape(rows, width * segs, nsrc // width)
    factor = 1.0 / math.sqrt(total_segs)
    totals = cross_terms(panel_own, white_all, factor)
    out = lax.psum_scatter(totals, "zhi", scatter_dimension=0, tiled=True)
    return out[:, :, :NB, :]


def solution(mesh):
    tm_size = mesh.shape["tm"]
    recv_size = mesh.shape["recv"]
    devices = np.asarray(mesh.devices).reshape(tm_size // 4, 2, 2, recv_size)
    inner = Mesh(devices, ("zhi", "zlo", "xlo", "recv"))
    return jax.shard_map(
        on_device,
        mesh=inner,
        in_specs=(P(("zhi", "zlo", "xlo"), "recv", None), P(("zhi", "zlo", "xlo"), "recv"), P()),
        out_specs=P(("zhi", "zlo", "xlo"), None, None, "recv"),
        check_vma=False,
    )
```

```python
import math

import jax
import jax.numpy as jnp
import numpy as np
from jax import lax
from jax.sharding import Mesh
from jax.sharding import PartitionSpec as P

NS = 2048
NB = 61
BIN0 = 40
NB_PAD = 64


def basis_table():
    sample_ids = np.arange(NS, dtype=np.int64)
    bin_ids = BIN0 + np.arange(NB, dtype=np.int64)
    phase_ids = (bin_ids[:, None] * sample_ids[None, :] % NS).astype(np.float32)
    angle = (np.float32(2.0 * math.pi / NS) * phase_ids).astype(np.float64)
    table = np.concatenate([np.cos(angle), -np.sin(angle)], axis=0).astype(np.float32)
    return jnp.asarray(table.astype(jnp.bfloat16))


def whiten_block(spec, valid_float):
    real_part = spec[:NB]
    imag_part = spec[NB:]
    power = real_part * real_part + imag_part * imag_part
    level = jnp.sum(power, axis=0) / (2.0 * NB)
    scale = lax.rsqrt(power + level[None] + 1e-06) * valid_float[None]
    return jnp.concatenate([real_part * scale, imag_part * scale], axis=0)


def pad_bins(part):
    return jnp.pad(part, [(0, NB_PAD - NB)] + [(0, 0)] * (part.ndim - 1))


def cross_terms(panel, white, factor):
    high = lax.Precision.HIGHEST
    src_real = pad_bins(panel[:NB])
    src_imag = pad_bins(panel[NB:])
    own_real = pad_bins(white[:NB])
    own_imag = pad_bins(white[NB:])
    real_sum = jnp.einsum("fts,ftc->sfc", src_real, own_real, precision=high) + jnp.einsum(
        "fts,ftc->sfc", src_imag, own_imag, precision=high
    )
    imag_sum = jnp.einsum("fts,ftc->sfc", src_real, own_imag, precision=high) - jnp.einsum(
        "fts,ftc->sfc", src_imag, own_real, precision=high
    )
    return jnp.stack([real_sum, imag_sum], axis=1) * factor


def psum_recv(value, size, passengers, hold_bit):
    bit = 1
    while bit < size:
        if bit == hold_bit:
            value, passengers = lax.optimization_barrier((value, passengers))
        pairs = [(i, i ^ bit) for i in range(size)]
        value = value + lax.ppermute(value, "recv", pairs)
        bit *= 2
    return value, passengers


def on_device(traces, valid, src_idx):
    seg_count = traces.shape[0]
    chan_count = traces.shape[1]
    group = ("zlo", "xlo")
    width = lax.axis_size("zlo") * lax.axis_size("xlo")
    total_segs = seg_count * width * lax.axis_size("zhi")
    basis = basis_table()
    valid_float = valid.astype(jnp.float32)
    offset = lax.axis_index("recv") * chan_count
    onehot = (src_idx[:, None] == offset + jnp.arange(chan_count, dtype=jnp.int32)[None, :]).astype(
        jnp.float32
    )
    spec = lax.dot_general(
        basis, traces, (((1,), (2,)), ((), ())), preferred_element_type=jnp.float32
    )
    white = whiten_block(spec, valid_float)
    q = lax.axis_index("zlo") * lax.axis_size("xlo") + lax.axis_index("xlo")
    moves = [[(r, r ^ b) for r in range(width)] for b in range(1, width)]
    white_parts = [lax.ppermute(white, group, pairs) for pairs in moves]
    partial_value = jnp.einsum("ktc,sc->kts", white, onehot, precision=lax.Precision.HIGHEST)
    panel, white_parts = psum_recv(
        partial_value, lax.axis_size("recv"), white_parts, lax.axis_size("recv") // 2
    )
    white_all = jnp.concatenate([white] + white_parts, axis=1)
    rows, segs, nsrc = panel.shape
    panel = panel.reshape(rows, segs, nsrc // width, width).transpose(3, 0, 1, 2)
    panel = lax.all_to_all(panel, group, 0, 0, tiled=True)
    blocks = [lax.dynamic_index_in_dim(panel, q ^ b, axis=0, keepdims=False) for b in range(width)]
    panel_own = jnp.concatenate(blocks, axis=1)
    factor = 1.0 / math.sqrt(total_segs)
    totals = cross_terms(panel_own, white_all, factor)
    out = lax.psum_scatter(totals, "zhi", scatter_dimension=0, tiled=True)
    return out[:, :, :NB, :]


def solution(mesh):
    tm_size = mesh.shape["tm"]
    recv_size = mesh.shape["recv"]
    devices = np.asarray(mesh.devices).reshape(tm_size // 4, 2, 2, recv_size)
    inner = Mesh(devices, ("zhi", "zlo", "xlo", "recv"))
    return jax.shard_map(
        on_device,
        mesh=inner,
        in_specs=(P(("zhi", "zlo", "xlo"), "recv", None), P(("zhi", "zlo", "xlo"), "recv"), P()),
        out_specs=P(("zhi", "zlo", "xlo"), None, None, "recv"),
        check_vma=False,
    )
```

```python
import math

import jax
import jax.numpy as jnp
import numpy as np
from jax import lax
from jax.sharding import Mesh
from jax.sharding import PartitionSpec as P

NS = 2048
NB = 61
BIN0 = 40
NB_PAD = 64


def basis_table():
    sample_ids = np.arange(NS, dtype=np.int64)
    bin_ids = BIN0 + np.arange(NB, dtype=np.int64)
    phase_ids = (bin_ids[:, None] * sample_ids[None, :] % NS).astype(np.float32)
    angle = (np.float32(2.0 * math.pi / NS) * phase_ids).astype(np.float64)
    table = np.concatenate([np.cos(angle), -np.sin(angle)], axis=0).astype(np.float32)
    return jnp.asarray(table.astype(jnp.bfloat16))


def whiten_block(spec, valid_float):
    real_part = spec[:NB]
    imag_part = spec[NB:]
    power = real_part * real_part + imag_part * imag_part
    level = jnp.sum(power, axis=0) / (2.0 * NB)
    scale = lax.rsqrt(power + level[None] + 1e-06) * valid_float[None]
    return jnp.concatenate([real_part * scale, imag_part * scale], axis=0)


def pad_bins(part):
    return jnp.pad(part, [(0, NB_PAD - NB)] + [(0, 0)] * (part.ndim - 1))


def cross_terms(panel, white, factor):
    high = lax.Precision.HIGHEST
    src_real = pad_bins(panel[:NB])
    src_imag = pad_bins(panel[NB:])
    own_real = pad_bins(white[:NB])
    own_imag = pad_bins(white[NB:])
    real_sum = jnp.einsum("fts,ftc->sfc", src_real, own_real, precision=high) + jnp.einsum(
        "fts,ftc->sfc", src_imag, own_imag, precision=high
    )
    imag_sum = jnp.einsum("fts,ftc->sfc", src_real, own_imag, precision=high) - jnp.einsum(
        "fts,ftc->sfc", src_imag, own_real, precision=high
    )
    return jnp.stack([real_sum, imag_sum], axis=1) * factor


def psum_recv(value, size, passengers, hold_bit):
    bit = 1
    while bit < size:
        if bit == hold_bit:
            value, passengers = lax.optimization_barrier((value, passengers))
        pairs = [(i, i ^ bit) for i in range(size)]
        value = value + lax.ppermute(value, "recv", pairs)
        bit *= 2
    return value, passengers


def on_device(traces, valid, src_idx):
    seg_count = traces.shape[0]
    chan_count = traces.shape[1]
    group = ("zlo", "xlo")
    width = lax.axis_size("zlo") * lax.axis_size("xlo")
    total_segs = seg_count * width * lax.axis_size("zhi")
    basis = basis_table()
    valid_float = valid.astype(jnp.float32)
    offset = lax.axis_index("recv") * chan_count
    onehot = (src_idx[:, None] == offset + jnp.arange(chan_count, dtype=jnp.int32)[None, :]).astype(
        jnp.float32
    )
    spec = lax.dot_general(
        basis, traces, (((1,), (2,)), ((), ())), preferred_element_type=jnp.float32
    )
    white = whiten_block(spec, valid_float)
    spread = jnp.broadcast_to(white[None], (width,) + white.shape)
    white_parts = lax.all_to_all(spread, group, 0, 0, tiled=True)
    partial_value = jnp.einsum("ktc,sc->kts", white, onehot, precision=lax.Precision.HIGHEST)
    panel, white_parts = psum_recv(
        partial_value, lax.axis_size("recv"), white_parts, lax.axis_size("recv") // 2
    )
    rows, segs, nchan = white.shape
    white_all = white_parts.transpose(1, 0, 2, 3).reshape(rows, width * segs, nchan)
    nsrc = panel.shape[2]
    panel = panel.reshape(rows, segs, nsrc // width, width).transpose(3, 0, 1, 2)
    panel = lax.all_to_all(panel, group, 0, 0, tiled=True)
    panel_own = panel.transpose(1, 0, 2, 3).reshape(rows, width * segs, nsrc // width)
    factor = 1.0 / math.sqrt(total_segs)
    totals = cross_terms(panel_own, white_all, factor)
    out = lax.psum_scatter(totals, "zhi", scatter_dimension=0, tiled=True)
    return out[:, :, :NB, :]


def solution(mesh):
    tm_size = mesh.shape["tm"]
    recv_size = mesh.shape["recv"]
    devices = np.asarray(mesh.devices).reshape(tm_size // 4, 2, 2, recv_size)
    inner = Mesh(devices, ("zhi", "zlo", "xlo", "recv"))
    return jax.shard_map(
        on_device,
        mesh=inner,
        in_specs=(P(("zhi", "zlo", "xlo"), "recv", None), P(("zhi", "zlo", "xlo"), "recv"), P()),
        out_specs=P(("zhi", "zlo", "xlo"), None, None, "recv"),
        check_vma=False,
    )
```

```python
import math

import jax
import jax.numpy as jnp
import numpy as np
from jax import lax
from jax.sharding import Mesh
from jax.sharding import PartitionSpec as P

NS = 2048
NB = 61
BIN0 = 40
NB_PAD = 64


def basis_table():
    sample_ids = np.arange(NS, dtype=np.int64)
    bin_ids = BIN0 + np.arange(NB, dtype=np.int64)
    phase_ids = (bin_ids[:, None] * sample_ids[None, :] % NS).astype(np.float32)
    angle = (np.float32(2.0 * math.pi / NS) * phase_ids).astype(np.float64)
    table = np.concatenate([np.cos(angle), -np.sin(angle)], axis=0).astype(np.float32)
    return jnp.asarray(table.astype(jnp.bfloat16))


def whiten_block(spec, valid_float):
    real_part = spec[:NB]
    imag_part = spec[NB:]
    power = real_part * real_part + imag_part * imag_part
    level = jnp.sum(power, axis=0) / (2.0 * NB)
    scale = lax.rsqrt(power + level[None] + 1e-06) * valid_float[None]
    return jnp.concatenate([real_part * scale, imag_part * scale], axis=0)


def pad_bins(part):
    return jnp.pad(part, [(0, NB_PAD - NB)] + [(0, 0)] * (part.ndim - 1))


def cross_terms(panel, white, factor):
    high = lax.Precision.HIGHEST
    src_real = pad_bins(panel[:NB])
    src_imag = pad_bins(panel[NB:])
    own_real = pad_bins(white[:NB])
    own_imag = pad_bins(white[NB:])
    real_sum = jnp.einsum("fts,ftc->sfc", src_real, own_real, precision=high) + jnp.einsum(
        "fts,ftc->sfc", src_imag, own_imag, precision=high
    )
    imag_sum = jnp.einsum("fts,ftc->sfc", src_real, own_imag, precision=high) - jnp.einsum(
        "fts,ftc->sfc", src_imag, own_real, precision=high
    )
    return jnp.stack([real_sum, imag_sum], axis=1) * factor


def psum_recv(value, size, passengers, hold_bit):
    bit = 1
    while bit < size:
        if bit == hold_bit:
            value, passengers = lax.optimization_barrier((value, passengers))
        pairs = [(i, i ^ bit) for i in range(size)]
        value = value + lax.ppermute(value, "recv", pairs)
        bit *= 2
    return value, passengers


def on_device(traces, valid, src_idx):
    seg_count = traces.shape[0]
    chan_count = traces.shape[1]
    group = ("zlo", "xlo")
    width = lax.axis_size("zlo") * lax.axis_size("xlo")
    total_segs = seg_count * width * lax.axis_size("zhi")
    basis = basis_table()
    valid_float = valid.astype(jnp.float32)
    offset = lax.axis_index("recv") * chan_count
    onehot = (src_idx[:, None] == offset + jnp.arange(chan_count, dtype=jnp.int32)[None, :]).astype(
        jnp.float32
    )
    spec = lax.dot_general(
        basis, traces, (((1,), (2,)), ((), ())), preferred_element_type=jnp.float32
    )
    white = whiten_block(spec, valid_float)
    rows, segs, nchan = white.shape
    spread = jnp.broadcast_to(white[:, None], (rows, width, segs, nchan)).reshape(rows, width * segs, nchan)
    white_parts = lax.all_to_all(spread, group, 1, 1, tiled=True)
    partial_value = jnp.einsum("ktc,sc->kts", white, onehot, precision=lax.Precision.HIGHEST)
    panel, white_parts = psum_recv(
        partial_value, lax.axis_size("recv"), white_parts, lax.axis_size("recv") // 2
    )
    white_all = white_parts
    nsrc = panel.shape[2]
    panel = panel.reshape(rows, segs, nsrc // width, width).transpose(0, 3, 1, 2)
    panel = panel.reshape(rows, width * segs, nsrc // width)
    panel_own = lax.all_to_all(panel, group, 1, 1, tiled=True)
    factor = 1.0 / math.sqrt(total_segs)
    totals = cross_terms(panel_own, white_all, factor)
    out = lax.psum_scatter(totals, "zhi", scatter_dimension=0, tiled=True)
    return out[:, :, :NB, :]


def solution(mesh):
    tm_size = mesh.shape["tm"]
    recv_size = mesh.shape["recv"]
    devices = np.asarray(mesh.devices).reshape(tm_size // 4, 2, 2, recv_size)
    inner = Mesh(devices, ("zhi", "zlo", "xlo", "recv"))
    return jax.shard_map(
        on_device,
        mesh=inner,
        in_specs=(P(("zhi", "zlo", "xlo"), "recv", None), P(("zhi", "zlo", "xlo"), "recv"), P()),
        out_specs=P(("zhi", "zlo", "xlo"), None, None, "recv"),
        check_vma=False,
    )
```

```python
import math

import jax
import jax.numpy as jnp
import numpy as np
from jax import lax
from jax.sharding import Mesh
from jax.sharding import PartitionSpec as P

NS = 2048
NB = 61
BIN0 = 40
NB_PAD = 64


def basis_table():
    sample_ids = np.arange(NS, dtype=np.int64)
    bin_ids = BIN0 + np.arange(NB, dtype=np.int64)
    phase_ids = (bin_ids[:, None] * sample_ids[None, :] % NS).astype(np.float32)
    angle = (np.float32(2.0 * math.pi / NS) * phase_ids).astype(np.float64)
    table = np.concatenate([np.cos(angle), -np.sin(angle)], axis=0).astype(np.float32)
    return jnp.asarray(table.astype(jnp.bfloat16))


def whiten_block(spec, valid_float):
    real_part = spec[:NB]
    imag_part = spec[NB:]
    power = real_part * real_part + imag_part * imag_part
    level = jnp.sum(power, axis=0) / (2.0 * NB)
    scale = lax.rsqrt(power + level[None] + 1e-06) * valid_float[None]
    return jnp.concatenate([real_part * scale, imag_part * scale], axis=0)


def pad_bins(part):
    return jnp.pad(part, [(0, NB_PAD - NB)] + [(0, 0)] * (part.ndim - 1))


def cross_terms(panel, white, factor):
    high = lax.Precision.HIGHEST
    src_real = pad_bins(panel[:NB])
    src_imag = pad_bins(panel[NB:])
    own_real = pad_bins(white[:NB])
    own_imag = pad_bins(white[NB:])
    real_sum = jnp.einsum("fts,ftc->sfc", src_real, own_real, precision=high) + jnp.einsum(
        "fts,ftc->sfc", src_imag, own_imag, precision=high
    )
    imag_sum = jnp.einsum("fts,ftc->sfc", src_real, own_imag, precision=high) - jnp.einsum(
        "fts,ftc->sfc", src_imag, own_real, precision=high
    )
    return jnp.stack([real_sum, imag_sum], axis=1) * factor


def psum_recv(value, size, passengers):
    bit = 1
    while bit < size:
        pairs = [(i, i ^ bit) for i in range(size)]
        value = value + lax.ppermute(value, "recv", pairs)
        bit *= 2
    return lax.optimization_barrier((value, passengers))


def on_device(traces, valid, src_idx):
    seg_count = traces.shape[0]
    chan_count = traces.shape[1]
    group = ("zlo", "xlo")
    width = lax.axis_size("zlo") * lax.axis_size("xlo")
    total_segs = seg_count * width * lax.axis_size("zhi")
    basis = basis_table()
    valid_float = valid.astype(jnp.float32)
    offset = lax.axis_index("recv") * chan_count
    onehot = (src_idx[:, None] == offset + jnp.arange(chan_count, dtype=jnp.int32)[None, :]).astype(
        jnp.float32
    )
    spec = lax.dot_general(
        basis, traces, (((1,), (2,)), ((), ())), preferred_element_type=jnp.float32
    )
    white = whiten_block(spec, valid_float)
    spread = jnp.broadcast_to(white[None], (width,) + white.shape)
    white_parts = lax.all_to_all(spread, group, 0, 0, tiled=True)
    partial_value = jnp.einsum("ktc,sc->kts", white, onehot, precision=lax.Precision.HIGHEST)
    panel, white_parts = psum_recv(partial_value, lax.axis_size("recv"), white_parts)
    rows, segs, nchan = white.shape
    white_all = white_parts.transpose(1, 0, 2, 3).reshape(rows, width * segs, nchan)
    nsrc = panel.shape[2]
    panel = panel.reshape(rows, segs, nsrc // width, width).transpose(3, 0, 1, 2)
    panel = lax.all_to_all(panel, group, 0, 0, tiled=True)
    panel_own = panel.transpose(1, 0, 2, 3).reshape(rows, width * segs, nsrc // width)
    factor = 1.0 / math.sqrt(total_segs)
    totals = cross_terms(panel_own, white_all, factor)
    out = lax.psum_scatter(totals, "zhi", scatter_dimension=0, tiled=True)
    return out[:, :, :NB, :]


def solution(mesh):
    tm_size = mesh.shape["tm"]
    recv_size = mesh.shape["recv"]
    devices = np.asarray(mesh.devices).reshape(tm_size // 4, 2, 2, recv_size)
    inner = Mesh(devices, ("zhi", "zlo", "xlo", "recv"))
    return jax.shard_map(
        on_device,
        mesh=inner,
        in_specs=(P(("zhi", "zlo", "xlo"), "recv", None), P(("zhi", "zlo", "xlo"), "recv"), P()),
        out_specs=P(("zhi", "zlo", "xlo"), None, None, "recv"),
        check_vma=False,
    )
```

```python
import math

import jax
import jax.numpy as jnp
import numpy as np
from jax import lax
from jax.sharding import Mesh
from jax.sharding import PartitionSpec as P

NS = 2048
NB = 61
BIN0 = 40


def basis_table():
    sample_ids = np.arange(NS, dtype=np.int64)
    bin_ids = BIN0 + np.arange(NB, dtype=np.int64)
    phase_ids = (bin_ids[:, None] * sample_ids[None, :] % NS).astype(np.float32)
    angle = (np.float32(2.0 * math.pi / NS) * phase_ids).astype(np.float64)
    table = np.concatenate([np.cos(angle), -np.sin(angle)], axis=0).astype(np.float32)
    return jnp.asarray(table.astype(jnp.bfloat16))


def whiten_block(spec, valid_float):
    real_part = spec[:NB]
    imag_part = spec[NB:]
    power = real_part * real_part + imag_part * imag_part
    level = jnp.sum(power, axis=0) / (2.0 * NB)
    scale = lax.rsqrt(power + level[None] + 1e-06) * valid_float[None]
    return jnp.concatenate([real_part * scale, imag_part * scale], axis=0)


def cross_terms(panel, white, factor):
    high = lax.Precision.HIGHEST
    src_real = panel[:NB]
    src_imag = panel[NB:]
    own_real = white[:NB]
    own_imag = white[NB:]
    real_sum = jnp.einsum("fts,ftc->sfc", src_real, own_real, precision=high) + jnp.einsum(
        "fts,ftc->sfc", src_imag, own_imag, precision=high
    )
    imag_sum = jnp.einsum("fts,ftc->sfc", src_real, own_imag, precision=high) - jnp.einsum(
        "fts,ftc->sfc", src_imag, own_real, precision=high
    )
    return jnp.stack([real_sum, imag_sum], axis=1) * factor


def psum_recv(value, size, passengers):
    bit = 1
    while bit < size:
        pairs = [(i, i ^ bit) for i in range(size)]
        value = value + lax.ppermute(value, "recv", pairs)
        bit *= 2
    return lax.optimization_barrier((value, passengers))


def on_device(traces, valid, src_idx):
    seg_count = traces.shape[0]
    chan_count = traces.shape[1]
    group = ("zlo", "xlo")
    width = lax.axis_size("zlo") * lax.axis_size("xlo")
    total_segs = seg_count * width * lax.axis_size("zhi")
    basis = basis_table()
    valid_float = valid.astype(jnp.float32)
    offset = lax.axis_index("recv") * chan_count
    onehot = (src_idx[:, None] == offset + jnp.arange(chan_count, dtype=jnp.int32)[None, :]).astype(
        jnp.float32
    )
    spec = lax.dot_general(
        basis, traces, (((1,), (2,)), ((), ())), preferred_element_type=jnp.float32
    )
    white = whiten_block(spec, valid_float)
    spread = jnp.broadcast_to(white[None], (width,) + white.shape)
    white_parts = lax.all_to_all(spread, group, 0, 0, tiled=True)
    partial_value = jnp.einsum("ktc,sc->kts", white, onehot, precision=lax.Precision.HIGHEST)
    panel, white_parts = psum_recv(partial_value, lax.axis_size("recv"), white_parts)
    rows, segs, nchan = white.shape
    white_all = white_parts.transpose(1, 0, 2, 3).reshape(rows, width * segs, nchan)
    nsrc = panel.shape[2]
    panel = panel.reshape(rows, segs, nsrc // width, width).transpose(3, 0, 1, 2)
    panel = lax.all_to_all(panel, group, 0, 0, tiled=True)
    panel_own = panel.transpose(1, 0, 2, 3).reshape(rows, width * segs, nsrc // width)
    factor = 1.0 / math.sqrt(total_segs)
    totals = cross_terms(panel_own, white_all, factor)
    arrived = lax.all_to_all(totals, "zhi", 0, 0, tiled=True)
    return jnp.sum(arrived, axis=0, keepdims=True)


def solution(mesh):
    tm_size = mesh.shape["tm"]
    recv_size = mesh.shape["recv"]
    devices = np.asarray(mesh.devices).reshape(tm_size // 4, 2, 2, recv_size)
    inner = Mesh(devices, ("zhi", "zlo", "xlo", "recv"))
    return jax.shard_map(
        on_device,
        mesh=inner,
        in_specs=(P(("zhi", "zlo", "xlo"), "recv", None), P(("zhi", "zlo", "xlo"), "recv"), P()),
        out_specs=P(("zhi", "zlo", "xlo"), None, None, "recv"),
        check_vma=False,
    )
```

```python
import math

import jax
import jax.numpy as jnp
import numpy as np
from jax import lax
from jax.sharding import Mesh
from jax.sharding import PartitionSpec as P

NS = 2048
NB = 61
BIN0 = 40


def basis_table():
    sample_ids = np.arange(NS, dtype=np.int64)
    bin_ids = BIN0 + np.arange(NB, dtype=np.int64)
    phase_ids = (bin_ids[:, None] * sample_ids[None, :] % NS).astype(np.float32)
    angle = (np.float32(2.0 * math.pi / NS) * phase_ids).astype(np.float64)
    table = np.concatenate([np.cos(angle), -np.sin(angle)], axis=0).astype(np.float32)
    return jnp.asarray(table.astype(jnp.bfloat16))


def whiten_block(spec, valid_float):
    real_part = spec[:NB]
    imag_part = spec[NB:]
    power = real_part * real_part + imag_part * imag_part
    level = jnp.sum(power, axis=0) / (2.0 * NB)
    scale = lax.rsqrt(power + level[None] + 1e-06) * valid_float[None]
    return jnp.concatenate([real_part * scale, imag_part * scale], axis=0)


def cross_terms(panel, white, factor):
    high = lax.Precision.HIGHEST
    src_real = panel[:NB]
    src_imag = panel[NB:]
    own_real = white[:NB]
    own_imag = white[NB:]
    real_sum = jnp.einsum("fts,ftc->sfc", src_real, own_real, precision=high) + jnp.einsum(
        "fts,ftc->sfc", src_imag, own_imag, precision=high
    )
    imag_sum = jnp.einsum("fts,ftc->sfc", src_real, own_imag, precision=high) - jnp.einsum(
        "fts,ftc->sfc", src_imag, own_real, precision=high
    )
    return jnp.stack([real_sum, imag_sum], axis=1) * factor


def psum_recv(value, size, passengers):
    bit = 1
    while bit < size:
        pairs = [(i, i ^ bit) for i in range(size)]
        value = value + lax.ppermute(value, "recv", pairs)
        bit *= 2
    return lax.optimization_barrier((value, passengers))


def on_device(traces, valid, src_idx):
    seg_count = traces.shape[0]
    chan_count = traces.shape[1]
    group = ("zlo", "xlo")
    width = lax.axis_size("zlo") * lax.axis_size("xlo")
    total_segs = seg_count * width * lax.axis_size("zhi")
    basis = basis_table()
    valid_float = valid.astype(jnp.float32)
    offset = lax.axis_index("recv") * chan_count
    onehot = (src_idx[:, None] == offset + jnp.arange(chan_count, dtype=jnp.int32)[None, :]).astype(
        jnp.float32
    )
    spec = lax.dot_general(
        basis, traces, (((1,), (2,)), ((), ())), preferred_element_type=jnp.float32
    )
    white = whiten_block(spec, valid_float)
    spread = jnp.broadcast_to(white[None], (width,) + white.shape)
    white_parts = lax.all_to_all(spread, group, 0, 0, tiled=True)
    partial_value = jnp.einsum("ktc,sc->kts", white, onehot, precision=lax.Precision.HIGHEST)
    panel, white_parts = psum_recv(partial_value, lax.axis_size("recv"), white_parts)
    rows, segs, nchan = white.shape
    white_all = white_parts.transpose(1, 0, 2, 3).reshape(rows, width * segs, nchan)
    nsrc = panel.shape[2]
    panel = panel.reshape(rows, segs, nsrc // width, width).transpose(3, 0, 1, 2)
    panel = lax.all_to_all(panel, group, 0, 0, tiled=True)
    panel_own = panel.transpose(1, 0, 2, 3).reshape(rows, width * segs, nsrc // width)
    factor = 1.0 / math.sqrt(total_segs)
    totals = cross_terms(panel_own, white_all, factor)
    arrived = lax.all_to_all(totals, "zhi", 0, 0, tiled=True)
    total = arrived[0:1]
    for k in range(1, arrived.shape[0]):
        total = total + arrived[k : k + 1]
    return total


def solution(mesh):
    tm_size = mesh.shape["tm"]
    recv_size = mesh.shape["recv"]
    devices = np.asarray(mesh.devices).reshape(tm_size // 4, 2, 2, recv_size)
    inner = Mesh(devices, ("zhi", "zlo", "xlo", "recv"))
    return jax.shard_map(
        on_device,
        mesh=inner,
        in_specs=(P(("zhi", "zlo", "xlo"), "recv", None), P(("zhi", "zlo", "xlo"), "recv"), P()),
        out_specs=P(("zhi", "zlo", "xlo"), None, None, "recv"),
        check_vma=False,
    )
```

```python
import math

import jax
import jax.numpy as jnp
import numpy as np
from jax import lax
from jax.sharding import Mesh
from jax.sharding import PartitionSpec as P

NS = 2048
NB = 61
BIN0 = 40


def basis_table():
    sample_ids = np.arange(NS, dtype=np.int64)
    bin_ids = BIN0 + np.arange(NB, dtype=np.int64)
    phase_ids = (bin_ids[:, None] * sample_ids[None, :] % NS).astype(np.float32)
    angle = (np.float32(2.0 * math.pi / NS) * phase_ids).astype(np.float64)
    table = np.concatenate([np.cos(angle), -np.sin(angle)], axis=0).astype(np.float32)
    return jnp.asarray(table.astype(jnp.bfloat16))


def whiten_block(spec, valid):
    real_part = spec[:NB]
    imag_part = spec[NB:]
    power = real_part * real_part + imag_part * imag_part
    level = jnp.sum(power, axis=0) / (2.0 * NB)
    scale = jnp.where(valid[None] != 0, lax.rsqrt(power + level[None] + 1e-06), 0.0)
    return jnp.concatenate([real_part * scale, imag_part * scale], axis=0)


def cross_terms(panel, white, factor):
    high = lax.Precision.HIGHEST
    src_real = panel[:NB]
    src_imag = panel[NB:]
    own_real = white[:NB]
    own_imag = white[NB:]
    real_sum = jnp.einsum("fts,ftc->sfc", src_real, own_real, precision=high) + jnp.einsum(
        "fts,ftc->sfc", src_imag, own_imag, precision=high
    )
    imag_sum = jnp.einsum("fts,ftc->sfc", src_real, own_imag, precision=high) - jnp.einsum(
        "fts,ftc->sfc", src_imag, own_real, precision=high
    )
    return jnp.stack([real_sum, imag_sum], axis=1) * factor


def psum_recv(value, size, passengers):
    bit = 1
    while bit < size:
        pairs = [(i, i ^ bit) for i in range(size)]
        value = value + lax.ppermute(value, "recv", pairs)
        bit *= 2
    return lax.optimization_barrier((value, passengers))


def on_device(traces, valid, src_idx):
    seg_count = traces.shape[0]
    chan_count = traces.shape[1]
    group = ("zlo", "xlo")
    width = lax.axis_size("zlo") * lax.axis_size("xlo")
    total_segs = seg_count * width * lax.axis_size("zhi")
    basis = basis_table()
    offset = lax.axis_index("recv") * chan_count
    onehot = (src_idx[:, None] == offset + jnp.arange(chan_count, dtype=jnp.int32)[None, :]).astype(
        jnp.float32
    )
    spec = lax.dot_general(
        basis, traces, (((1,), (2,)), ((), ())), preferred_element_type=jnp.float32
    )
    white = whiten_block(spec, valid)
    spread = jnp.broadcast_to(white[None], (width,) + white.shape)
    white_parts = lax.all_to_all(spread, group, 0, 0, tiled=True)
    partial_value = jnp.einsum("ktc,sc->kts", white, onehot, precision=lax.Precision.HIGHEST)
    panel, white_parts = psum_recv(partial_value, lax.axis_size("recv"), white_parts)
    rows, segs, nchan = white.shape
    white_all = white_parts.transpose(1, 0, 2, 3).reshape(rows, width * segs, nchan)
    nsrc = panel.shape[2]
    panel = panel.reshape(rows, segs, nsrc // width, width).transpose(3, 0, 1, 2)
    panel = lax.all_to_all(panel, group, 0, 0, tiled=True)
    panel_own = panel.transpose(1, 0, 2, 3).reshape(rows, width * segs, nsrc // width)
    factor = 1.0 / math.sqrt(total_segs)
    totals = cross_terms(panel_own, white_all, factor)
    arrived = lax.all_to_all(totals, "zhi", 0, 0, tiled=True)
    total = arrived[0:1]
    for k in range(1, arrived.shape[0]):
        total = total + arrived[k : k + 1]
    return total


def solution(mesh):
    tm_size = mesh.shape["tm"]
    recv_size = mesh.shape["recv"]
    devices = np.asarray(mesh.devices).reshape(tm_size // 4, 2, 2, recv_size)
    inner = Mesh(devices, ("zhi", "zlo", "xlo", "recv"))
    return jax.shard_map(
        on_device,
        mesh=inner,
        in_specs=(P(("zhi", "zlo", "xlo"), "recv", None), P(("zhi", "zlo", "xlo"), "recv"), P()),
        out_specs=P(("zhi", "zlo", "xlo"), None, None, "recv"),
        check_vma=False,
    )
```

```python
import math

import jax
import jax.numpy as jnp
import numpy as np
from jax import lax
from jax.sharding import Mesh
from jax.sharding import PartitionSpec as P

NS = 2048
NB = 61
BIN0 = 40


def basis_table():
    sample_ids = np.arange(NS, dtype=np.int64)
    bin_ids = BIN0 + np.arange(NB, dtype=np.int64)
    phase_ids = (bin_ids[:, None] * sample_ids[None, :] % NS).astype(np.float32)
    angle = (np.float32(2.0 * math.pi / NS) * phase_ids).astype(np.float64)
    table = np.concatenate([np.cos(angle), -np.sin(angle)], axis=0).astype(np.float32)
    return jnp.asarray(table.astype(jnp.bfloat16))


def whiten_block(spec, valid_float):
    real_part = spec[:NB]
    imag_part = spec[NB:]
    power = real_part * real_part + imag_part * imag_part
    level = jnp.sum(power, axis=0) / (2.0 * NB)
    scale = lax.rsqrt(power + level[None] + 1e-06) * valid_float[None]
    return jnp.concatenate([real_part * scale, imag_part * scale], axis=0)


def cross_terms(panel, white, factor):
    high = lax.Precision.HIGHEST
    src_real = panel[:NB]
    src_imag = panel[NB:]
    own_real = white[:NB]
    own_imag = white[NB:]
    real_sum = jnp.einsum("fts,ftc->sfc", src_real, own_real, precision=high) + jnp.einsum(
        "fts,ftc->sfc", src_imag, own_imag, precision=high
    )
    imag_sum = jnp.einsum("fts,ftc->sfc", src_real, own_imag, precision=high) - jnp.einsum(
        "fts,ftc->sfc", src_imag, own_real, precision=high
    )
    return jnp.concatenate([real_sum, imag_sum], axis=1) * factor


def psum_recv(value, size, passengers):
    bit = 1
    while bit < size:
        pairs = [(i, i ^ bit) for i in range(size)]
        value = value + lax.ppermute(value, "recv", pairs)
        bit *= 2
    return lax.optimization_barrier((value, passengers))


def on_device(traces, valid, src_idx):
    seg_count = traces.shape[0]
    chan_count = traces.shape[1]
    group = ("zlo", "xlo")
    width = lax.axis_size("zlo") * lax.axis_size("xlo")
    total_segs = seg_count * width * lax.axis_size("zhi")
    basis = basis_table()
    valid_float = valid.astype(jnp.float32)
    offset = lax.axis_index("recv") * chan_count
    onehot = (src_idx[:, None] == offset + jnp.arange(chan_count, dtype=jnp.int32)[None, :]).astype(
        jnp.float32
    )
    spec = lax.dot_general(
        basis, traces, (((1,), (2,)), ((), ())), preferred_element_type=jnp.float32
    )
    white = whiten_block(spec, valid_float)
    spread = jnp.broadcast_to(white[None], (width,) + white.shape)
    white_parts = lax.all_to_all(spread, group, 0, 0, tiled=True)
    partial_value = jnp.einsum("ktc,sc->kts", white, onehot, precision=lax.Precision.HIGHEST)
    panel, white_parts = psum_recv(partial_value, lax.axis_size("recv"), white_parts)
    rows, segs, nchan = white.shape
    white_all = white_parts.transpose(1, 0, 2, 3).reshape(rows, width * segs, nchan)
    nsrc = panel.shape[2]
    panel = panel.reshape(rows, segs, nsrc // width, width).transpose(3, 0, 1, 2)
    panel = lax.all_to_all(panel, group, 0, 0, tiled=True)
    panel_own = panel.transpose(1, 0, 2, 3).reshape(rows, width * segs, nsrc // width)
    factor = 1.0 / math.sqrt(total_segs)
    totals = cross_terms(panel_own, white_all, factor)
    arrived = lax.all_to_all(totals, "zhi", 0, 0, tiled=True)
    total = arrived[0:1]
    for k in range(1, arrived.shape[0]):
        total = total + arrived[k : k + 1]
    return total.reshape(1, 2, NB, total.shape[2])


def solution(mesh):
    tm_size = mesh.shape["tm"]
    recv_size = mesh.shape["recv"]
    devices = np.asarray(mesh.devices).reshape(tm_size // 4, 2, 2, recv_size)
    inner = Mesh(devices, ("zhi", "zlo", "xlo", "recv"))
    return jax.shard_map(
        on_device,
        mesh=inner,
        in_specs=(P(("zhi", "zlo", "xlo"), "recv", None), P(("zhi", "zlo", "xlo"), "recv"), P()),
        out_specs=P(("zhi", "zlo", "xlo"), None, None, "recv"),
        check_vma=False,
    )
```

```python
import math

import jax
import jax.numpy as jnp
import numpy as np
from jax import lax
from jax.sharding import Mesh
from jax.sharding import PartitionSpec as P

NS = 2048
NB = 61
BIN0 = 40


def basis_table():
    sample_ids = np.arange(NS, dtype=np.int64)
    bin_ids = BIN0 + np.arange(NB, dtype=np.int64)
    phase_ids = (bin_ids[:, None] * sample_ids[None, :] % NS).astype(np.float32)
    angle = (np.float32(2.0 * math.pi / NS) * phase_ids).astype(np.float64)
    table = np.concatenate([np.cos(angle), -np.sin(angle)], axis=0).astype(np.float32)
    return jnp.asarray(table.astype(jnp.bfloat16))


def whiten_block(spec, valid_float):
    real_part = spec[:NB]
    imag_part = spec[NB:]
    power = real_part * real_part + imag_part * imag_part
    level = jnp.sum(power, axis=0) / (2.0 * NB)
    scale = lax.rsqrt(power + level[None] + 1e-06) * valid_float[None]
    return jnp.concatenate([real_part * scale, imag_part * scale], axis=0)


def cross_terms(panel, white, factor):
    high = lax.Precision.HIGH
    src_real = panel[:NB]
    src_imag = panel[NB:]
    own_real = white[:NB]
    own_imag = white[NB:]
    real_sum = jnp.einsum("fts,ftc->sfc", src_real, own_real, precision=high) + jnp.einsum(
        "fts,ftc->sfc", src_imag, own_imag, precision=high
    )
    imag_sum = jnp.einsum("fts,ftc->sfc", src_real, own_imag, precision=high) - jnp.einsum(
        "fts,ftc->sfc", src_imag, own_real, precision=high
    )
    return jnp.stack([real_sum, imag_sum], axis=1) * factor


def psum_recv(value, size, passengers):
    bit = 1
    while bit < size:
        pairs = [(i, i ^ bit) for i in range(size)]
        value = value + lax.ppermute(value, "recv", pairs)
        bit *= 2
    return lax.optimization_barrier((value, passengers))


def on_device(traces, valid, src_idx):
    seg_count = traces.shape[0]
    chan_count = traces.shape[1]
    group = ("zlo", "xlo")
    width = lax.axis_size("zlo") * lax.axis_size("xlo")
    total_segs = seg_count * width * lax.axis_size("zhi")
    basis = basis_table()
    valid_float = valid.astype(jnp.float32)
    offset = lax.axis_index("recv") * chan_count
    onehot = (src_idx[:, None] == offset + jnp.arange(chan_count, dtype=jnp.int32)[None, :]).astype(
        jnp.float32
    )
    spec = lax.dot_general(
        basis, traces, (((1,), (2,)), ((), ())), preferred_element_type=jnp.float32
    )
    white = whiten_block(spec, valid_float)
    spread = jnp.broadcast_to(white[None], (width,) + white.shape)
    white_parts = lax.all_to_all(spread, group, 0, 0, tiled=True)
    partial_value = jnp.einsum("ktc,sc->kts", white, onehot, precision=lax.Precision.HIGHEST)
    panel, white_parts = psum_recv(partial_value, lax.axis_size("recv"), white_parts)
    rows, segs, nchan = white.shape
    white_all = white_parts.transpose(1, 0, 2, 3).reshape(rows, width * segs, nchan)
    nsrc = panel.shape[2]
    panel = panel.reshape(rows, segs, nsrc // width, width).transpose(3, 0, 1, 2)
    panel = lax.all_to_all(panel, group, 0, 0, tiled=True)
    panel_own = panel.transpose(1, 0, 2, 3).reshape(rows, width * segs, nsrc // width)
    factor = 1.0 / math.sqrt(total_segs)
    totals = cross_terms(panel_own, white_all, factor)
    arrived = lax.all_to_all(totals, "zhi", 0, 0, tiled=True)
    total = arrived[0:1]
    for k in range(1, arrived.shape[0]):
        total = total + arrived[k : k + 1]
    return total


def solution(mesh):
    tm_size = mesh.shape["tm"]
    recv_size = mesh.shape["recv"]
    devices = np.asarray(mesh.devices).reshape(tm_size // 4, 2, 2, recv_size)
    inner = Mesh(devices, ("zhi", "zlo", "xlo", "recv"))
    return jax.shard_map(
        on_device,
        mesh=inner,
        in_specs=(P(("zhi", "zlo", "xlo"), "recv", None), P(("zhi", "zlo", "xlo"), "recv"), P()),
        out_specs=P(("zhi", "zlo", "xlo"), None, None, "recv"),
        check_vma=False,
    )
```

```python
import math

import jax
import jax.numpy as jnp
import numpy as np
from jax import lax
from jax.sharding import Mesh
from jax.sharding import PartitionSpec as P

NS = 2048
NB = 61
BIN0 = 40


def basis_table():
    sample_ids = np.arange(NS, dtype=np.int64)
    bin_ids = BIN0 + np.arange(NB, dtype=np.int64)
    phase_ids = (bin_ids[:, None] * sample_ids[None, :] % NS).astype(np.float32)
    angle = (np.float32(2.0 * math.pi / NS) * phase_ids).astype(np.float64)
    table = np.concatenate([np.cos(angle), -np.sin(angle)], axis=0).astype(np.float32)
    return jnp.asarray(table.astype(jnp.bfloat16))


def whiten_block(spec, valid_float):
    real_part = spec[:NB]
    imag_part = spec[NB:]
    power = real_part * real_part + imag_part * imag_part
    level = jnp.sum(power, axis=0) / (2.0 * NB)
    scale = lax.rsqrt(power + level[None] + 1e-06) * valid_float[None]
    return jnp.concatenate([real_part * scale, imag_part * scale], axis=0)


def cross_terms(panel, white, factor):
    high = lax.Precision.HIGH
    src_real = panel[:NB]
    src_imag = panel[NB:]
    own_real = white[:NB]
    own_imag = white[NB:]
    src_both = jnp.concatenate([src_real, src_imag], axis=1)
    src_flip = jnp.concatenate([src_real, -src_imag], axis=1)
    own_both = jnp.concatenate([own_real, own_imag], axis=1)
    own_swap = jnp.concatenate([own_imag, own_real], axis=1)
    real_sum = jnp.einsum("fts,ftc->sfc", src_both, own_both, precision=high)
    imag_sum = jnp.einsum("fts,ftc->sfc", src_flip, own_swap, precision=high)
    return jnp.stack([real_sum, imag_sum], axis=1) * factor


def psum_recv(value, size, passengers):
    bit = 1
    while bit < size:
        pairs = [(i, i ^ bit) for i in range(size)]
        value = value + lax.ppermute(value, "recv", pairs)
        bit *= 2
    return lax.optimization_barrier((value, passengers))


def on_device(traces, valid, src_idx):
    seg_count = traces.shape[0]
    chan_count = traces.shape[1]
    group = ("zlo", "xlo")
    width = lax.axis_size("zlo") * lax.axis_size("xlo")
    total_segs = seg_count * width * lax.axis_size("zhi")
    basis = basis_table()
    valid_float = valid.astype(jnp.float32)
    offset = lax.axis_index("recv") * chan_count
    onehot = (src_idx[:, None] == offset + jnp.arange(chan_count, dtype=jnp.int32)[None, :]).astype(
        jnp.float32
    )
    spec = lax.dot_general(
        basis, traces, (((1,), (2,)), ((), ())), preferred_element_type=jnp.float32
    )
    white = whiten_block(spec, valid_float)
    spread = jnp.broadcast_to(white[None], (width,) + white.shape)
    white_parts = lax.all_to_all(spread, group, 0, 0, tiled=True)
    partial_value = jnp.einsum("ktc,sc->kts", white, onehot, precision=lax.Precision.HIGHEST)
    panel, white_parts = psum_recv(partial_value, lax.axis_size("recv"), white_parts)
    rows, segs, nchan = white.shape
    white_all = white_parts.transpose(1, 0, 2, 3).reshape(rows, width * segs, nchan)
    nsrc = panel.shape[2]
    panel = panel.reshape(rows, segs, nsrc // width, width).transpose(3, 0, 1, 2)
    panel = lax.all_to_all(panel, group, 0, 0, tiled=True)
    panel_own = panel.transpose(1, 0, 2, 3).reshape(rows, width * segs, nsrc // width)
    factor = 1.0 / math.sqrt(total_segs)
    totals = cross_terms(panel_own, white_all, factor)
    arrived = lax.all_to_all(totals, "zhi", 0, 0, tiled=True)
    total = arrived[0:1]
    for k in range(1, arrived.shape[0]):
        total = total + arrived[k : k + 1]
    return total


def solution(mesh):
    tm_size = mesh.shape["tm"]
    recv_size = mesh.shape["recv"]
    devices = np.asarray(mesh.devices).reshape(tm_size // 4, 2, 2, recv_size)
    inner = Mesh(devices, ("zhi", "zlo", "xlo", "recv"))
    return jax.shard_map(
        on_device,
        mesh=inner,
        in_specs=(P(("zhi", "zlo", "xlo"), "recv", None), P(("zhi", "zlo", "xlo"), "recv"), P()),
        out_specs=P(("zhi", "zlo", "xlo"), None, None, "recv"),
        check_vma=False,
    )
```

```python
import math

import jax
import jax.numpy as jnp
import numpy as np
from jax import lax
from jax.sharding import Mesh
from jax.sharding import PartitionSpec as P

NS = 2048
NB = 61
BIN0 = 40


def basis_table():
    sample_ids = np.arange(NS, dtype=np.int64)
    bin_ids = BIN0 + np.arange(NB, dtype=np.int64)
    phase_ids = (bin_ids[:, None] * sample_ids[None, :] % NS).astype(np.float32)
    angle = (np.float32(2.0 * math.pi / NS) * phase_ids).astype(np.float64)
    table = np.concatenate([np.cos(angle), -np.sin(angle)], axis=0).astype(np.float32)
    return jnp.asarray(table.astype(jnp.bfloat16))


def whiten_block(spec, valid_float):
    real_part = spec[:NB]
    imag_part = spec[NB:]
    power = real_part * real_part + imag_part * imag_part
    level = jnp.sum(power, axis=0) / (2.0 * NB)
    scale = lax.rsqrt(power + level[None] + 1e-06) * valid_float[None]
    return jnp.concatenate([real_part * scale, imag_part * scale], axis=0)


def cross_terms(panel, white, factor):
    high = lax.Precision.HIGH
    src_real = panel[:NB]
    src_imag = panel[NB:]
    own_real = white[:NB]
    own_imag = white[NB:]
    src_both = jnp.concatenate([src_real, src_imag], axis=1)
    src_flip = jnp.concatenate([src_real, -src_imag], axis=1)
    own_both = jnp.concatenate([own_real, own_imag], axis=1)
    own_swap = jnp.concatenate([own_imag, own_real], axis=1)
    real_sum = jnp.einsum("fts,ftc->sfc", src_both, own_both, precision=high)
    imag_sum = jnp.einsum("fts,ftc->sfc", src_flip, own_swap, precision=high)
    return jnp.stack([real_sum, imag_sum], axis=1) * factor


def psum_recv(value, size, passengers):
    bit = 1
    while bit < size:
        pairs = [(i, i ^ bit) for i in range(size)]
        value = value + lax.ppermute(value, "recv", pairs)
        bit *= 2
    return lax.optimization_barrier((value, passengers))


def on_device(traces, valid, src_idx):
    seg_count = traces.shape[0]
    chan_count = traces.shape[1]
    group = ("zlo", "xlo")
    width = lax.axis_size("zlo") * lax.axis_size("xlo")
    total_segs = seg_count * width * lax.axis_size("zhi")
    basis = basis_table()
    valid_float = valid.astype(jnp.float32)
    offset = lax.axis_index("recv") * chan_count
    onehot = (src_idx[:, None] == offset + jnp.arange(chan_count, dtype=jnp.int32)[None, :]).astype(
        jnp.float32
    )
    spec = lax.dot_general(
        basis, traces, (((1,), (2,)), ((), ())), preferred_element_type=jnp.float32
    )
    white = whiten_block(spec, valid_float)
    spread = jnp.broadcast_to(white[None], (width,) + white.shape)
    white_parts = lax.all_to_all(spread, group, 0, 0, tiled=True)
    nsrc = onehot.shape[0]
    onehot = onehot.reshape(nsrc // width, width, chan_count).transpose(1, 0, 2)
    partial_value = jnp.einsum("ktc,rsc->rkts", white, onehot, precision=lax.Precision.HIGHEST)
    panel, white_parts = psum_recv(partial_value, lax.axis_size("recv"), white_parts)
    rows, segs, nchan = white.shape
    white_all = white_parts.transpose(1, 0, 2, 3).reshape(rows, width * segs, nchan)
    panel = lax.all_to_all(panel, group, 0, 0, tiled=True)
    panel_own = panel.transpose(1, 0, 2, 3).reshape(rows, width * segs, nsrc // width)
    factor = 1.0 / math.sqrt(total_segs)
    totals = cross_terms(panel_own, white_all, factor)
    arrived = lax.all_to_all(totals, "zhi", 0, 0, tiled=True)
    total = arrived[0:1]
    for k in range(1, arrived.shape[0]):
        total = total + arrived[k : k + 1]
    return total


def solution(mesh):
    tm_size = mesh.shape["tm"]
    recv_size = mesh.shape["recv"]
    devices = np.asarray(mesh.devices).reshape(tm_size // 4, 2, 2, recv_size)
    inner = Mesh(devices, ("zhi", "zlo", "xlo", "recv"))
    return jax.shard_map(
        on_device,
        mesh=inner,
        in_specs=(P(("zhi", "zlo", "xlo"), "recv", None), P(("zhi", "zlo", "xlo"), "recv"), P()),
        out_specs=P(("zhi", "zlo", "xlo"), None, None, "recv"),
        check_vma=False,
    )
```

```python
import math

import jax
import jax.numpy as jnp
import numpy as np
from jax import lax
from jax.sharding import Mesh
from jax.sharding import PartitionSpec as P

NS = 2048
NB = 61
BIN0 = 40


def basis_table():
    sample_ids = np.arange(NS, dtype=np.int64)
    bin_ids = BIN0 + np.arange(NB, dtype=np.int64)
    phase_ids = (bin_ids[:, None] * sample_ids[None, :] % NS).astype(np.float32)
    angle = (np.float32(2.0 * math.pi / NS) * phase_ids).astype(np.float64)
    table = np.concatenate([np.cos(angle), -np.sin(angle)], axis=0).astype(np.float32)
    return jnp.asarray(table.astype(jnp.bfloat16))


def whiten_block(spec, valid_float):
    real_part = spec[:NB]
    imag_part = spec[NB:]
    power = real_part * real_part + imag_part * imag_part
    level = jnp.sum(power, axis=0) / (2.0 * NB)
    scale = lax.rsqrt(power + level[None] + 1e-06) * valid_float[None]
    return jnp.concatenate([real_part * scale, imag_part * scale], axis=0)


def cross_terms(panel, white, factor):
    high = lax.Precision.HIGH
    src_real = panel[:NB]
    src_imag = panel[NB:]
    own_real = white[:NB]
    own_imag = white[NB:]
    src_both = jnp.concatenate([src_real, src_imag], axis=1)
    src_flip = jnp.concatenate([src_real, -src_imag], axis=1)
    own_both = jnp.concatenate([own_real, own_imag], axis=1)
    own_swap = jnp.concatenate([own_imag, own_real], axis=1)
    real_sum = jnp.einsum("fts,ftc->sfc", src_both, own_both, precision=high)
    imag_sum = jnp.einsum("fts,ftc->sfc", src_flip, own_swap, precision=high)
    return jnp.stack([real_sum, imag_sum], axis=1) * factor


def psum_recv(value, size, passengers):
    bit = 1
    while bit < size:
        pairs = [(i, i ^ bit) for i in range(size)]
        value = value + lax.ppermute(value, "recv", pairs)
        bit *= 2
    return lax.optimization_barrier((value, passengers))


def on_device(traces, valid, src_idx):
    seg_count = traces.shape[0]
    chan_count = traces.shape[1]
    group = ("zlo", "xlo")
    width = lax.axis_size("zlo") * lax.axis_size("xlo")
    total_segs = seg_count * width * lax.axis_size("zhi")
    basis = basis_table()
    valid_float = valid.astype(jnp.float32)
    offset = lax.axis_index("recv") * chan_count
    onehot = (src_idx[:, None] == offset + jnp.arange(chan_count, dtype=jnp.int32)[None, :]).astype(
        jnp.float32
    )
    spec = lax.dot_general(
        basis, traces, (((1,), (2,)), ((), ())), preferred_element_type=jnp.float32
    )
    white = whiten_block(spec, valid_float)
    spread = jnp.broadcast_to(white[None], (width,) + white.shape)
    white_parts = lax.all_to_all(spread, group, 0, 0, tiled=True)
    nsrc = onehot.shape[0]
    onehot = onehot.reshape(nsrc // width, width, chan_count).transpose(1, 0, 2)
    partial_value = jnp.einsum("ktc,rsc->rkts", white, onehot, precision=lax.Precision.HIGH)
    panel, white_parts = psum_recv(partial_value, lax.axis_size("recv"), white_parts)
    rows, segs, nchan = white.shape
    white_all = white_parts.transpose(1, 0, 2, 3).reshape(rows, width * segs, nchan)
    panel = lax.all_to_all(panel, group, 0, 0, tiled=True)
    panel_own = panel.transpose(1, 0, 2, 3).reshape(rows, width * segs, nsrc // width)
    factor = 1.0 / math.sqrt(total_segs)
    totals = cross_terms(panel_own, white_all, factor)
    arrived = lax.all_to_all(totals, "zhi", 0, 0, tiled=True)
    total = arrived[0:1]
    for k in range(1, arrived.shape[0]):
        total = total + arrived[k : k + 1]
    return total


def solution(mesh):
    tm_size = mesh.shape["tm"]
    recv_size = mesh.shape["recv"]
    devices = np.asarray(mesh.devices).reshape(tm_size // 4, 2, 2, recv_size)
    inner = Mesh(devices, ("zhi", "zlo", "xlo", "recv"))
    return jax.shard_map(
        on_device,
        mesh=inner,
        in_specs=(P(("zhi", "zlo", "xlo"), "recv", None), P(("zhi", "zlo", "xlo"), "recv"), P()),
        out_specs=P(("zhi", "zlo", "xlo"), None, None, "recv"),
        check_vma=False,
    )
```
